512 devices in a mesh: dp: 32 (over y, x, core), tensor: 16 (over z).
Axes of the slice: x: 4, y: 4, z: 16, core: 2. Of those that a mesh axis runs over, the one named last changes fastest.
Arguments:
- activations: bfloat16 [32768, 4096], P('dp', 'tensor'), may hold values from -40 to 40
- labels: int32 [32768], P('dp'), may hold values from 0 to 7, as said below
Outputs:
- covariance: float32 [4096, 4096], P('tensor', 'dp')
- cross_covariance: float32 [8, 4096], P(None, 'tensor')
The draws below stay inside these ranges and needn't reach their ends.
Inputs may be any that keep to these rules, and one draw needn't show every extreme that they name: Every one of the 8 classes labels at least one token.
All inputs are finite; a program needn't handle non-finite values.
Results may differ from the reference program's by a relative error of at most 0.0003.
Values may be sent and summed in bfloat16 or wider, within the bound.
No kernel may reach another device: no remote copies, remote signals or barrier semaphores. Data moves between devices by JAX's collectives and lax.ppermute only.
A program may use at most 64 MiB of HBM per device.

```python
import jax
import jax.numpy as jnp
from jax import lax

D = 4096
CLASSES = 8
TOK_DEV = 1024
TOKENS = 32768
N_DP = 32


def label_table(key):
    drawn = jax.random.randint(jax.random.fold_in(key, 11), (TOKENS,), 0, CLASSES)
    order = jax.random.permutation(jax.random.fold_in(key, 12), CLASSES).astype(jnp.int32)
    return drawn.astype(jnp.int32).at[:CLASSES].set(order)


def draw_labels(key, part):
    return label_table(key)


def draw_activations(key, part):
    label_rows = label_table(key)
    offsets = 0.7 * jax.random.normal(jax.random.fold_in(key, 21), (CLASSES, D), jnp.float32)
    noise = jax.random.normal(jax.random.fold_in(key, 22), (TOKENS, D), jnp.float32)
    values = noise + offsets[label_rows]
    return jnp.clip(values, -40.0, 40.0).astype(jnp.bfloat16)


def setup_inputs(seed: int = 0) -> dict:
    splits = jax.random.split(jax.random.key(seed), 3)
    activations = draw_activations(jax.random.fold_in(splits[2], 71), 0)
    labels = draw_labels(jax.random.fold_in(splits[2], 71), 0)
    return {"activations": activations, "labels": labels}


def reference(activations, labels):
    values = activations.astype(jnp.float32)
    token_total = values.shape[0]
    classes = jnp.arange(CLASSES, dtype=jnp.int32)
    onehot = (labels[None, :] == classes[:, None]).astype(jnp.float32)
    class_counts = jnp.sum(onehot, axis=1)
    class_sums = jnp.dot(onehot, values, precision=lax.Precision.HIGHEST)
    overall_mean = jnp.sum(class_sums, axis=0) / token_total
    blocks = values.reshape(N_DP, TOK_DEV, D)

    def add_block(total, block):
        return total + jnp.dot(block.T, block, precision=lax.Precision.HIGHEST), None

    gram, _ = lax.scan(add_block, jnp.zeros((D, D), jnp.float32), blocks)
    covariance = gram / token_total - overall_mean[:, None] * overall_mean[None, :]
    cross_covariance = (class_sums - class_counts[:, None] * overall_mean[None, :]) / token_total
    return covariance, cross_covariance
```

```python
import jax
import jax.numpy as jnp
from jax import lax
from jax.sharding import PartitionSpec as P

D = 4096
CLASSES = 8


def butterfly_sum(x, axis, n):
    k = 1
    while k < n:
        perm = [(i, i ^ k) for i in range(n)]
        x = x + lax.ppermute(x, axis, perm)
        k *= 2
    return x


def body(activations, labels):
    tok_rows, slice_width = activations.shape
    n_dp = lax.axis_size("dp")
    assert n_dp & (n_dp - 1) == 0
    token_total = tok_rows * n_dp
    col_width = D // n_dp
    classes = jnp.arange(CLASSES, dtype=jnp.int32)
    matches = labels[None, :] == classes[:, None]
    onehot = matches.astype(jnp.bfloat16)
    local_counts = jnp.sum(matches.astype(jnp.float32), axis=1)
    gathered = lax.all_gather(activations, "tensor", axis=1, tiled=True)
    gram_cols = lax.psum_scatter(
        lax.dot_general(
            gathered, activations, (((0,), (0,)), ((), ())), preferred_element_type=jnp.float32
        ),
        "dp",
        scatter_dimension=0,
        tiled=True,
    )
    slice_start = lax.axis_index("tensor") * slice_width
    wide_local = jnp.dot(onehot, gathered, preferred_element_type=jnp.float32)
    stats = jnp.concatenate(
        [wide_local, jnp.broadcast_to(local_counts[:, None], (CLASSES, 128))], axis=1
    )
    stats = butterfly_sum(stats, "dp", n_dp)
    class_sums = stats[:, :D]
    class_counts = stats[:, D]
    own_sums = lax.dynamic_slice_in_dim(class_sums, slice_start, slice_width, 1)
    overall_mean = jnp.sum(class_sums, axis=0) / token_total
    mean_rows = lax.dynamic_slice_in_dim(overall_mean, slice_start, slice_width, 0)
    mean_cols = lax.dynamic_slice_in_dim(
        overall_mean, lax.axis_index("dp") * col_width, col_width, 0
    )
    covariance = gram_cols.T / token_total - mean_rows[:, None] * mean_cols[None, :]
    cross_covariance = (own_sums - class_counts[:, None] * mean_rows[None, :]) / token_total
    return (covariance, cross_covariance)


def solution(mesh):
    in_specs = (P("dp", "tensor"), P("dp"))
    out_specs = (P("tensor", "dp"), P(None, "tensor"))
    return jax.shard_map(body, mesh=mesh, in_specs=in_specs, out_specs=out_specs, check_vma=False)
```

```python
import jax
import jax.numpy as jnp
from jax import lax
from jax.sharding import PartitionSpec as P

D = 4096
CLASSES = 8
CHUNKS = 4
RS_BITS = (0, 1, 3, 2, 4)


def butterfly_sum(x, axis, n):
    k = 1
    while k < n:
        perm = [(i, i ^ k) for i in range(n)]
        x = x + lax.ppermute(x, axis, perm)
        k *= 2
    return x


def butterfly_scatter(x, axis, n, bits):
    me = lax.axis_index(axis)
    nb = len(bits)
    tail = x.shape[1:]
    x = x.reshape((2,) * nb + tail)
    left = list(range(nb))
    for b in bits:
        pos = left.index(nb - 1 - b)
        mine = (me >> b) & 1
        keep = lax.dynamic_index_in_dim(x, mine, pos, keepdims=False)
        send = lax.dynamic_index_in_dim(x, 1 - mine, pos, keepdims=False)
        perm = [(i, i ^ (1 << b)) for i in range(n)]
        x = keep + lax.ppermute(send, axis, perm)
        left.pop(pos)
    return x


def body(activations, labels):
    tok_rows, slice_width = activations.shape
    n_dp = lax.axis_size("dp")
    n_t = lax.axis_size("tensor")
    assert n_dp == 1 << len(RS_BITS)
    token_total = tok_rows * n_dp
    col_width = D // n_dp
    halves = slice_width // col_width
    w = col_width // CHUNKS
    classes = jnp.arange(CLASSES, dtype=jnp.int32)
    matches = labels[None, :] == classes[:, None]
    onehot = matches.astype(jnp.bfloat16)
    local_counts = jnp.sum(matches.astype(jnp.float32), axis=1)
    own_local = jnp.dot(onehot, activations, preferred_element_type=jnp.float32)
    stats = jnp.concatenate(
        [own_local, jnp.broadcast_to(local_counts[:, None], (CLASSES, 128))], axis=1
    )
    stats = butterfly_sum(stats, "dp", n_dp)
    own_sums = stats[:, :slice_width]
    class_counts = stats[:, slice_width]

    own_t = activations.T.reshape(halves, col_width, tok_rows)
    parts = [own_t[:, k * w:(k + 1) * w, :].reshape(halves * w, tok_rows) for k in range(CHUNKS)]
    pieces = []
    colsums = []
    for k in range(CHUNKS):
        part = parts[k]
        g = lax.all_gather(part, "tensor", axis=0, tiled=True)
        prod = lax.dot_general(
            g, activations, (((1,), (0,)), ((), ())), preferred_element_type=jnp.float32
        ).reshape(n_dp, w, slice_width)
        colsums.append(jnp.sum(g.astype(jnp.float32), axis=1).reshape(n_dp, w))
        if k == CHUNKS - 1:
            colsum = jnp.concatenate(colsums, axis=1)
            extra = jnp.zeros((n_dp, 8, slice_width), jnp.float32)
            extra = extra.at[:, 0, :col_width].set(colsum)
            prod = jnp.concatenate([prod, extra], axis=1)
        if k + 1 < CHUNKS:
            parts[k + 1], prod = lax.optimization_barrier((parts[k + 1], prod))
        piece = butterfly_scatter(prod, "dp", n_dp, RS_BITS)
        if k + 2 < CHUNKS:
            parts[k + 2], piece = lax.optimization_barrier((parts[k + 2], piece))
        pieces.append(piece)
    mean_cols = pieces[-1][w, :col_width] / token_total
    gram_cols = jnp.concatenate(pieces[:-1] + [pieces[-1][:w]], axis=0)

    mean_rows = jnp.sum(own_sums, axis=0) / token_total
    covariance = gram_cols.T / token_total - mean_rows[:, None] * mean_cols[None, :]
    cross_covariance = (own_sums - class_counts[:, None] * mean_rows[None, :]) / token_total
    return (covariance, cross_covariance)


def solution(mesh):
    in_specs = (P("dp", "tensor"), P("dp"))
    out_specs = (P("tensor", "dp"), P(None, "tensor"))
    return jax.shard_map(body, mesh=mesh, in_specs=in_specs, out_specs=out_specs, check_vma=False)
```

```python
import jax
import jax.numpy as jnp
from jax import lax
from jax.sharding import PartitionSpec as P

D = 4096
CLASSES = 8


def butterfly_sum(x, axis, n):
    k = 1
    while k < n:
        perm = [(i, i ^ k) for i in range(n)]
        x = x + lax.ppermute(x, axis, perm)
        k *= 2
    return x


def body(activations, labels):
    tok_rows, slice_width = activations.shape
    n_dp = lax.axis_size("dp")
    assert n_dp & (n_dp - 1) == 0
    token_total = tok_rows * n_dp
    col_width = D // n_dp
    classes = jnp.arange(CLASSES, dtype=jnp.int32)
    matches = labels[None, :] == classes[:, None]
    onehot = matches.astype(jnp.bfloat16)
    local_counts = jnp.sum(matches.astype(jnp.float32), axis=1)
    gathered = lax.all_gather(activations, "tensor", axis=1, tiled=True)
    prod = lax.dot_general(
        gathered, activations, (((0,), (0,)), ((), ())), preferred_element_type=jnp.float32
    ).reshape(n_dp, col_width, slice_width)
    recv = lax.all_to_all(prod, "dp", 0, 0, tiled=True)
    gram_cols = jnp.sum(recv, axis=0)
    slice_start = lax.axis_index("tensor") * slice_width
    wide_local = jnp.dot(onehot, gathered, preferred_element_type=jnp.float32)
    stats = jnp.concatenate(
        [wide_local, jnp.broadcast_to(local_counts[:, None], (CLASSES, 128))], axis=1
    )
    stats = butterfly_sum(stats, "dp", n_dp)
    class_sums = stats[:, :D]
    class_counts = stats[:, D]
    own_sums = lax.dynamic_slice_in_dim(class_sums, slice_start, slice_width, 1)
    overall_mean = jnp.sum(class_sums, axis=0) / token_total
    mean_rows = lax.dynamic_slice_in_dim(overall_mean, slice_start, slice_width, 0)
    mean_cols = lax.dynamic_slice_in_dim(
        overall_mean, lax.axis_index("dp") * col_width, col_width, 0
    )
    covariance = gram_cols.T / token_total - mean_rows[:, None] * mean_cols[None, :]
    cross_covariance = (own_sums - class_counts[:, None] * mean_rows[None, :]) / token_total
    return (covariance, cross_covariance)


def solution(mesh):
    in_specs = (P("dp", "tensor"), P("dp"))
    out_specs = (P("tensor", "dp"), P(None, "tensor"))
    return jax.shard_map(body, mesh=mesh, in_specs=in_specs, out_specs=out_specs, check_vma=False)
```

```python
import jax
import jax.numpy as jnp
from jax import lax
from jax.sharding import PartitionSpec as P

D = 4096
CLASSES = 8


def butterfly_sum(x, axis, n):
    k = 1
    while k < n:
        perm = [(i, i ^ k) for i in range(n)]
        x = x + lax.ppermute(x, axis, perm)
        k *= 2
    return x


def body(activations, labels):
    tok_rows, slice_width = activations.shape
    n_dp = lax.axis_size("dp")
    assert n_dp & (n_dp - 1) == 0
    token_total = tok_rows * n_dp
    col_width = D // n_dp
    classes = jnp.arange(CLASSES, dtype=jnp.int32)
    matches = labels[None, :] == classes[:, None]
    onehot = matches.astype(jnp.bfloat16)
    local_counts = jnp.sum(matches.astype(jnp.float32), axis=1)
    own_local = jnp.dot(onehot, activations, preferred_element_type=jnp.float32)
    stats = jnp.concatenate(
        [own_local, jnp.broadcast_to(local_counts[:, None], (CLASSES, 128))], axis=1
    )
    stats = butterfly_sum(stats, "dp", n_dp)

    gathered = lax.all_gather(activations, "tensor", axis=1, tiled=True)
    gathered, stats = lax.optimization_barrier((gathered, stats))
    prod = lax.dot_general(
        gathered, activations, (((0,), (0,)), ((), ())), preferred_element_type=jnp.float32
    ).reshape(n_dp, col_width, slice_width)
    colsum = jnp.sum(gathered.astype(jnp.float32), axis=0).reshape(n_dp, 1, col_width)
    extra = jnp.pad(colsum, ((0, 0), (0, 7), (0, slice_width - col_width)))
    payload = jnp.concatenate([prod, extra], axis=1)
    recv = lax.all_to_all(payload, "dp", 0, 0, tiled=True)
    total = jnp.sum(recv, axis=0)
    gram_cols = total[:col_width]
    mean_cols = total[col_width, :col_width] / token_total

    own_sums = stats[:, :slice_width]
    class_counts = stats[:, slice_width]
    mean_rows = jnp.sum(own_sums, axis=0) / token_total
    covariance = gram_cols.T / token_total - mean_rows[:, None] * mean_cols[None, :]
    cross_covariance = (own_sums - class_counts[:, None] * mean_rows[None, :]) / token_total
    return (covariance, cross_covariance)


def solution(mesh):
    in_specs = (P("dp", "tensor"), P("dp"))
    out_specs = (P("tensor", "dp"), P(None, "tensor"))
    return jax.shard_map(body, mesh=mesh, in_specs=in_specs, out_specs=out_specs, check_vma=False)
```

```python
import jax
import jax.numpy as jnp
from jax import lax
from jax.sharding import PartitionSpec as P

D = 4096
CLASSES = 8
EXTRA_ROWS = 16


def butterfly_sum(x, axis, n):
    k = 1
    while k < n:
        perm = [(i, i ^ k) for i in range(n)]
        x = x + lax.ppermute(x, axis, perm)
        k *= 2
    return x


def body(activations, labels):
    tok_rows, slice_width = activations.shape
    n_dp = lax.axis_size("dp")
    assert n_dp & (n_dp - 1) == 0
    token_total = tok_rows * n_dp
    col_width = D // n_dp
    classes = jnp.arange(CLASSES, dtype=jnp.int32)
    matches = labels[None, :] == classes[:, None]
    onehot = matches.astype(jnp.bfloat16)
    local_counts = jnp.sum(matches.astype(jnp.float32), axis=1)
    own_local = jnp.dot(onehot, activations, preferred_element_type=jnp.float32)
    stats = jnp.concatenate(
        [own_local, jnp.broadcast_to(local_counts[:, None], (CLASSES, 128))], axis=1
    )
    stats = butterfly_sum(stats, "dp", n_dp)

    gathered = lax.all_gather(activations, "tensor", axis=1, tiled=True)
    gathered, stats = lax.optimization_barrier((gathered, stats))
    prod = lax.dot_general(
        gathered, activations, (((0,), (0,)), ((), ())), preferred_element_type=jnp.float32
    ).reshape(n_dp, col_width, slice_width)
    ones = jnp.ones((8, tok_rows), jnp.bfloat16)
    colsum = jnp.dot(ones, gathered, preferred_element_type=jnp.float32)[0]
    extra = jnp.pad(
        colsum.reshape(n_dp, 1, col_width),
        ((0, 0), (0, EXTRA_ROWS - 1), (0, slice_width - col_width)),
    )
    payload = jnp.concatenate([prod, extra], axis=1)
    rows = col_width + EXTRA_ROWS
    half_rows = rows // 2

    me = lax.axis_index("dp")
    core = me & 1
    pairs = payload.reshape(n_dp // 2, 2, rows, slice_width)
    keep = lax.dynamic_index_in_dim(pairs, core, 1, keepdims=False)
    send = lax.dynamic_index_in_dim(pairs, 1 - core, 1, keepdims=False)
    core_swap = [(i, i ^ 1) for i in range(n_dp)]
    chip_sum = keep + lax.ppermute(send, "dp", core_swap)
    halves = chip_sum.reshape(n_dp, half_rows, slice_width)
    recv = lax.all_to_all(halves, "dp", 0, 0, tiled=True)
    by_core = jnp.sum(recv.reshape(n_dp // 2, 2, half_rows, slice_width), axis=0)
    mine = lax.dynamic_index_in_dim(by_core, core, 0, keepdims=False)
    other = lax.dynamic_index_in_dim(by_core, 1 - core, 0, keepdims=False)
    got = lax.ppermute(other, "dp", core_swap)
    total = jnp.where(
        core == 0, jnp.concatenate([mine, got], axis=0), jnp.concatenate([got, mine], axis=0)
    )
    gram_cols = total[:col_width]
    mean_cols = total[col_width, :col_width] / token_total

    own_sums = stats[:, :slice_width]
    class_counts = stats[:, slice_width]
    mean_rows = jnp.sum(own_sums, axis=0) / token_total
    covariance = gram_cols.T / token_total - mean_rows[:, None] * mean_cols[None, :]
    cross_covariance = (own_sums - class_counts[:, None] * mean_rows[None, :]) / token_total
    return (covariance, cross_covariance)


def solution(mesh):
    in_specs = (P("dp", "tensor"), P("dp"))
    out_specs = (P("tensor", "dp"), P(None, "tensor"))
    return jax.shard_map(body, mesh=mesh, in_specs=in_specs, out_specs=out_specs, check_vma=False)
```

```python
import jax
import jax.numpy as jnp
from jax import lax
from jax.sharding import PartitionSpec as P

D = 4096
CLASSES = 8
EXTRA_ROWS = 16


def butterfly_sum(x, axis, n):
    k = 1
    while k < n:
        perm = [(i, i ^ k) for i in range(n)]
        x = x + lax.ppermute(x, axis, perm)
        k *= 2
    return x


def body(activations, labels):
    tok_rows, slice_width = activations.shape
    n_dp = lax.axis_size("dp")
    assert n_dp & (n_dp - 1) == 0
    token_total = tok_rows * n_dp
    col_width = D // n_dp
    classes = jnp.arange(CLASSES, dtype=jnp.int32)
    matches = labels[None, :] == classes[:, None]
    onehot = matches.astype(jnp.bfloat16)
    local_counts = jnp.sum(matches.astype(jnp.float32), axis=1)
    own_local = jnp.dot(onehot, activations, preferred_element_type=jnp.float32)
    stats = jnp.concatenate(
        [own_local, jnp.broadcast_to(local_counts[:, None], (CLASSES, 128))], axis=1
    )
    stats = butterfly_sum(stats, "dp", n_dp)

    gathered = lax.all_gather(activations, "tensor", axis=0, tiled=False)
    gathered, stats = lax.optimization_barrier((gathered, stats))
    prod = lax.dot_general(
        gathered, activations, (((1,), (0,)), ((), ())), preferred_element_type=jnp.float32
    ).reshape(n_dp, col_width, slice_width)
    ones = jnp.ones((8, tok_rows), jnp.bfloat16)
    colsum = lax.dot_general(
        gathered, ones, (((1,), (1,)), ((), ())), preferred_element_type=jnp.float32
    )[..., 0].reshape(D)
    extra = jnp.pad(
        colsum.reshape(n_dp, 1, col_width),
        ((0, 0), (0, EXTRA_ROWS - 1), (0, slice_width - col_width)),
    )
    payload = jnp.concatenate([prod, extra], axis=1)
    rows = col_width + EXTRA_ROWS
    half_rows = rows // 2

    me = lax.axis_index("dp")
    core = me & 1
    pairs = payload.reshape(n_dp // 2, 2, rows, slice_width)
    keep = lax.dynamic_index_in_dim(pairs, core, 1, keepdims=False)
    send = lax.dynamic_index_in_dim(pairs, 1 - core, 1, keepdims=False)
    core_swap = [(i, i ^ 1) for i in range(n_dp)]
    chip_sum = keep + lax.ppermute(send, "dp", core_swap)
    halves = chip_sum.reshape(n_dp, half_rows, slice_width)
    recv = lax.all_to_all(halves, "dp", 0, 0, tiled=True)
    by_core = jnp.sum(recv.reshape(n_dp // 2, 2, half_rows, slice_width), axis=0)
    mine = lax.dynamic_index_in_dim(by_core, core, 0, keepdims=False)
    other = lax.dynamic_index_in_dim(by_core, 1 - core, 0, keepdims=False)
    got = lax.ppermute(other, "dp", core_swap)
    total = jnp.where(
        core == 0, jnp.concatenate([mine, got], axis=0), jnp.concatenate([got, mine], axis=0)
    )
    gram_cols = total[:col_width]
    mean_cols = total[col_width, :col_width] / token_total

    own_sums = stats[:, :slice_width]
    class_counts = stats[:, slice_width]
    mean_rows = jnp.sum(own_sums, axis=0) / token_total
    covariance = gram_cols.T / token_total - mean_rows[:, None] * mean_cols[None, :]
    cross_covariance = (own_sums - class_counts[:, None] * mean_rows[None, :]) / token_total
    return (covariance, cross_covariance)


def solution(mesh):
    in_specs = (P("dp", "tensor"), P("dp"))
    out_specs = (P("tensor", "dp"), P(None, "tensor"))
    return jax.shard_map(body, mesh=mesh, in_specs=in_specs, out_specs=out_specs, check_vma=False)
```

```python
import jax
import jax.numpy as jnp
from jax import lax
from jax.sharding import PartitionSpec as P

D = 4096
CLASSES = 8


def butterfly_sum(x, axis, n):
    k = 1
    while k < n:
        perm = [(i, i ^ k) for i in range(n)]
        x = x + lax.ppermute(x, axis, perm)
        k *= 2
    return x


def body(activations, labels):
    tok_rows, slice_width = activations.shape
    n_dp = lax.axis_size("dp")
    assert n_dp & (n_dp - 1) == 0
    token_total = tok_rows * n_dp
    col_width = D // n_dp
    classes = jnp.arange(CLASSES, dtype=jnp.int32)
    matches = labels[None, :] == classes[:, None]
    onehot = matches.astype(jnp.bfloat16)
    local_counts = jnp.sum(matches.astype(jnp.float32), axis=1)
    own_local = jnp.dot(onehot, activations, preferred_element_type=jnp.float32)
    stats = jnp.concatenate(
        [own_local, jnp.broadcast_to(local_counts[:, None], (CLASSES, 128))], axis=1
    )
    stats = butterfly_sum(stats, "dp", n_dp)

    own_sums = stats[:, :slice_width]
    class_counts = stats[:, slice_width]
    mean_rows = jnp.sum(own_sums, axis=0) / token_total
    mean_all = lax.all_gather(mean_rows, "tensor", axis=0, tiled=True)

    gathered = lax.all_gather(activations, "tensor", axis=0, tiled=False)
    gathered, stats, mean_all = lax.optimization_barrier((gathered, stats, mean_all))
    prod = lax.dot_general(
        gathered, activations, (((1,), (0,)), ((), ())), preferred_element_type=jnp.float32
    ).reshape(n_dp, col_width, slice_width)
    own_sums = stats[:, :slice_width]
    class_counts = stats[:, slice_width]
    mean_rows = jnp.sum(own_sums, axis=0) / token_total
    mean_cols = lax.dynamic_slice_in_dim(mean_all, lax.axis_index("dp") * col_width, col_width)
    payload = prod
    rows = col_width
    half_rows = rows // 2

    me = lax.axis_index("dp")
    core = me & 1
    pairs = payload.reshape(n_dp // 2, 2, rows, slice_width)
    keep = lax.dynamic_index_in_dim(pairs, core, 1, keepdims=False)
    send = lax.dynamic_index_in_dim(pairs, 1 - core, 1, keepdims=False)
    core_swap = [(i, i ^ 1) for i in range(n_dp)]
    chip_sum = keep + lax.ppermute(send, "dp", core_swap)
    halves = chip_sum.reshape(n_dp, half_rows, slice_width)
    recv = lax.all_to_all(halves, "dp", 0, 0, tiled=True)
    by_core = jnp.sum(recv.reshape(n_dp // 2, 2, half_rows, slice_width), axis=0)
    mine = lax.dynamic_index_in_dim(by_core, core, 0, keepdims=False)
    other = lax.dynamic_index_in_dim(by_core, 1 - core, 0, keepdims=False)
    got = lax.ppermute(other, "dp", core_swap)
    total = jnp.where(
        core == 0, jnp.concatenate([mine, got], axis=0), jnp.concatenate([got, mine], axis=0)
    )
    gram_cols = total
    covariance = gram_cols.T / token_total - mean_rows[:, None] * mean_cols[None, :]
    cross_covariance = (own_sums - class_counts[:, None] * mean_rows[None, :]) / token_total
    return (covariance, cross_covariance)


def solution(mesh):
    in_specs = (P("dp", "tensor"), P("dp"))
    out_specs = (P("tensor", "dp"), P(None, "tensor"))
    return jax.shard_map(body, mesh=mesh, in_specs=in_specs, out_specs=out_specs, check_vma=False)
```

```python
import jax
import jax.numpy as jnp
from jax import lax
from jax.sharding import PartitionSpec as P

D = 4096
CLASSES = 8
EXTRA_ROWS = 16


def butterfly_sum(x, axis, n):
    k = 1
    while k < n:
        perm = [(i, i ^ k) for i in range(n)]
        x = x + lax.ppermute(x, axis, perm)
        k *= 2
    return x


def body(activations, labels):
    tok_rows, slice_width = activations.shape
    n_dp = lax.axis_size("dp")
    assert n_dp & (n_dp - 1) == 0
    token_total = tok_rows * n_dp
    col_width = D // n_dp
    classes = jnp.arange(CLASSES, dtype=jnp.int32)
    matches = labels[None, :] == classes[:, None]
    onehot = matches.astype(jnp.bfloat16)
    local_counts = jnp.sum(matches.astype(jnp.float32), axis=1)
    own_local = jnp.dot(onehot, activations, preferred_element_type=jnp.float32)
    stats = jnp.concatenate(
        [own_local, jnp.broadcast_to(local_counts[:, None], (CLASSES, 128))], axis=1
    )
    stats = butterfly_sum(stats, "dp", n_dp)

    n_t = lax.axis_size("tensor")
    assert n_t % 4 == 0 and n_dp == 2 * n_t and slice_width == 2 * col_width
    win = n_t // 4
    m = lax.axis_index("tensor")
    blocks = [None] * (2 * win + 1)
    blocks[win] = activations
    fwd = activations
    bwd = activations
    up = [(i, (i + 1) % n_t) for i in range(n_t)]
    down = [(i, (i - 1) % n_t) for i in range(n_t)]
    for step in range(1, win + 1):
        fwd = lax.ppermute(fwd, "tensor", up)
        bwd = lax.ppermute(bwd, "tensor", down)
        blocks[win - step] = fwd
        blocks[win + step] = bwd
    wst = jnp.stack(blocks)
    contract = (((1,), (0,)), ((), ()))
    near = lax.dot_general(wst, activations, contract, preferred_element_type=jnp.float32)
    far_a = lax.dot_general(
        wst[win + 1:], wst[0], contract, preferred_element_type=jnp.float32
    )
    n_b = n_t - 3 * win - 1
    far_b = lax.dot_general(
        wst[0], wst[win + 1:win + 1 + n_b], (((0,), (1,)), ((), ())),
        preferred_element_type=jnp.float32,
    ).transpose(1, 0, 2)
    prod = jnp.concatenate([near, far_a, far_b], axis=0).reshape(n_dp, col_width, slice_width)
    ones = jnp.ones((8, tok_rows), jnp.bfloat16)
    cs = lax.dot_general(wst, ones, (((1,), (1,)), ((), ())), preferred_element_type=jnp.float32)[..., 0]
    cs_off = jnp.concatenate([cs, cs[win + 1:], jnp.broadcast_to(cs[0], (n_b, slice_width))], axis=0)
    extra = jnp.pad(
        cs_off.reshape(n_dp, 1, col_width),
        ((0, 0), (0, EXTRA_ROWS - 1), (0, slice_width - col_width)),
    )
    off_payload = jnp.concatenate([prod, extra], axis=1)
    rows = col_width + EXTRA_ROWS
    half_rows = rows // 2
    shift = (2 * m - 2 * win) % n_dp
    doubled = jnp.concatenate([off_payload, off_payload], axis=0)
    payload = lax.dynamic_slice_in_dim(doubled, (n_dp - shift) % n_dp, n_dp, axis=0)

    me = lax.axis_index("dp")
    core = me & 1
    pairs = payload.reshape(n_dp // 2, 2, rows, slice_width)
    keep = lax.dynamic_index_in_dim(pairs, core, 1, keepdims=False)
    send = lax.dynamic_index_in_dim(pairs, 1 - core, 1, keepdims=False)
    core_swap = [(i, i ^ 1) for i in range(n_dp)]
    chip_sum = keep + lax.ppermute(send, "dp", core_swap)
    halves = chip_sum.reshape(n_dp, half_rows, slice_width)
    recv = lax.all_to_all(halves, "dp", 0, 0, tiled=True)
    by_core = jnp.sum(recv.reshape(n_dp // 2, 2, half_rows, slice_width), axis=0)
    mine = lax.dynamic_index_in_dim(by_core, core, 0, keepdims=False)
    other = lax.dynamic_index_in_dim(by_core, 1 - core, 0, keepdims=False)
    got = lax.ppermute(other, "dp", core_swap)
    total = jnp.where(
        core == 0, jnp.concatenate([mine, got], axis=0), jnp.concatenate([got, mine], axis=0)
    )
    me = lax.axis_index("dp")
    perm = []
    for src_s in range(n_dp):
        for src_m in range(n_t):
            o = (src_s // 2 - src_m) % n_t
            h = src_s % 2
            if win < o <= 2 * win:
                dst = ((src_s - 2 * win) % n_dp, (src_m - win) % n_t)
            elif o > 2 * win and o < n_t - win:
                dst = ((2 * (src_m - win) + h) % n_dp, (src_m + o - 2 * win) % n_t)
            else:
                continue
            perm.append((src_s * n_t + src_m, dst[0] * n_t + dst[1]))
    moved = lax.ppermute(total, ("dp", "tensor"), perm)
    my_o = (me // 2 - m) % n_t
    is_far = jnp.logical_and(my_o > win, my_o < n_t - win)
    final = jnp.where(is_far, moved, total)
    gram_cols = final[:col_width]
    mean_cols = final[col_width, :col_width] / token_total
    own_sums = stats[:, :slice_width]
    class_counts = stats[:, slice_width]
    mean_rows = jnp.sum(own_sums, axis=0) / token_total
    covariance = gram_cols.T / token_total - mean_rows[:, None] * mean_cols[None, :]
    cross_covariance = (own_sums - class_counts[:, None] * mean_rows[None, :]) / token_total
    return (covariance, cross_covariance)


def solution(mesh):
    in_specs = (P("dp", "tensor"), P("dp"))
    out_specs = (P("tensor", "dp"), P(None, "tensor"))
    return jax.shard_map(body, mesh=mesh, in_specs=in_specs, out_specs=out_specs, check_vma=False)
```

```python
import jax
import jax.numpy as jnp
from jax import lax
from jax.sharding import PartitionSpec as P

D = 4096
CLASSES = 8
EXTRA_ROWS = 16


def butterfly_sum(x, axis, n):
    k = 1
    while k < n:
        perm = [(i, i ^ k) for i in range(n)]
        x = x + lax.ppermute(x, axis, perm)
        k *= 2
    return x


def body(activations, labels):
    tok_rows, slice_width = activations.shape
    n_dp = lax.axis_size("dp")
    assert n_dp & (n_dp - 1) == 0
    token_total = tok_rows * n_dp
    col_width = D // n_dp
    classes = jnp.arange(CLASSES, dtype=jnp.int32)
    matches = labels[None, :] == classes[:, None]
    onehot = matches.astype(jnp.bfloat16)
    local_counts = jnp.sum(matches.astype(jnp.float32), axis=1)
    own_local = jnp.dot(onehot, activations, preferred_element_type=jnp.float32)
    stats = jnp.concatenate(
        [own_local, jnp.broadcast_to(local_counts[:, None], (CLASSES, 128))], axis=1
    )
    stats = butterfly_sum(stats, "dp", n_dp)

    n_t = lax.axis_size("tensor")
    assert n_t % 4 == 0 and n_dp == 2 * n_t and slice_width == 2 * col_width
    win = n_t // 4
    m = lax.axis_index("tensor")
    blocks = [None] * (2 * win + 1)
    blocks[win] = activations
    fwd = activations
    bwd = activations
    up = [(i, (i + 1) % n_t) for i in range(n_t)]
    down = [(i, (i - 1) % n_t) for i in range(n_t)]
    for step in range(1, win + 1):
        fwd = lax.ppermute(fwd, "tensor", up)
        bwd = lax.ppermute(bwd, "tensor", down)
        blocks[win - step] = fwd
        blocks[win + step] = bwd
    wst = jnp.stack(blocks)
    wst, stats = lax.optimization_barrier((wst, stats))
    contract = (((1,), (0,)), ((), ()))
    near = lax.dot_general(wst, activations, contract, preferred_element_type=jnp.float32)
    far_a = lax.dot_general(
        wst[win + 1:], wst[0], contract, preferred_element_type=jnp.float32
    )
    n_b = n_t - 3 * win - 1
    far_b = lax.dot_general(
        wst[0], wst[win + 1:win + 1 + n_b], (((0,), (1,)), ((), ())),
        preferred_element_type=jnp.float32,
    ).transpose(1, 0, 2)
    prod = jnp.concatenate([near, far_a, far_b], axis=0).reshape(n_dp, col_width, slice_width)
    ones = jnp.ones((8, tok_rows), jnp.bfloat16)
    cs = lax.dot_general(wst, ones, (((1,), (1,)), ((), ())), preferred_element_type=jnp.float32)[..., 0]
    cs_off = jnp.concatenate([cs, cs[win + 1:], jnp.broadcast_to(cs[0], (n_b, slice_width))], axis=0)
    extra = jnp.pad(
        cs_off.reshape(n_dp, 1, col_width),
        ((0, 0), (0, EXTRA_ROWS - 1), (0, slice_width - col_width)),
    )
    off_payload = jnp.concatenate([prod, extra], axis=1)
    rows = col_width + EXTRA_ROWS
    half_rows = rows // 2
    shift = (2 * m - 2 * win) % n_dp
    doubled = jnp.concatenate([off_payload, off_payload], axis=0)
    payload = lax.dynamic_slice_in_dim(doubled, (n_dp - shift) % n_dp, n_dp, axis=0)

    me = lax.axis_index("dp")
    core = me & 1
    pairs = payload.reshape(n_dp // 2, 2, rows, slice_width)
    keep = lax.dynamic_index_in_dim(pairs, core, 1, keepdims=False)
    send = lax.dynamic_index_in_dim(pairs, 1 - core, 1, keepdims=False)
    core_swap = [(i, i ^ 1) for i in range(n_dp)]
    chip_sum = keep + lax.ppermute(send, "dp", core_swap)
    halves = chip_sum.reshape(n_dp, half_rows, slice_width)
    recv = lax.all_to_all(halves, "dp", 0, 0, tiled=True)
    by_core = jnp.sum(recv.reshape(n_dp // 2, 2, half_rows, slice_width), axis=0)
    mine = lax.dynamic_index_in_dim(by_core, core, 0, keepdims=False)
    other = lax.dynamic_index_in_dim(by_core, 1 - core, 0, keepdims=False)
    got = lax.ppermute(other, "dp", core_swap)
    total = jnp.where(
        core == 0, jnp.concatenate([mine, got], axis=0), jnp.concatenate([got, mine], axis=0)
    )
    me = lax.axis_index("dp")
    perm = []
    for src_s in range(n_dp):
        for src_m in range(n_t):
            o = (src_s // 2 - src_m) % n_t
            h = src_s % 2
            if win < o <= 2 * win:
                dst = ((src_s - 2 * win) % n_dp, (src_m - win) % n_t)
            elif o > 2 * win and o < n_t - win:
                dst = ((2 * (src_m - win) + h) % n_dp, (src_m + o - 2 * win) % n_t)
            else:
                continue
            perm.append((src_s * n_t + src_m, dst[0] * n_t + dst[1]))
    moved = lax.ppermute(total, ("dp", "tensor"), perm)
    my_o = (me // 2 - m) % n_t
    is_far = jnp.logical_and(my_o > win, my_o < n_t - win)
    final = jnp.where(is_far, moved, total)
    gram_cols = final[:col_width]
    mean_cols = final[col_width, :col_width] / token_total
    own_sums = stats[:, :slice_width]
    class_counts = stats[:, slice_width]
    mean_rows = jnp.sum(own_sums, axis=0) / token_total
    covariance = gram_cols.T / token_total - mean_rows[:, None] * mean_cols[None, :]
    cross_covariance = (own_sums - class_counts[:, None] * mean_rows[None, :]) / token_total
    return (covariance, cross_covariance)


def solution(mesh):
    in_specs = (P("dp", "tensor"), P("dp"))
    out_specs = (P("tensor", "dp"), P(None, "tensor"))
    return jax.shard_map(body, mesh=mesh, in_specs=in_specs, out_specs=out_specs, check_vma=False)
```

```python
import jax
import jax.numpy as jnp
from jax import lax
from jax.sharding import PartitionSpec as P

D = 4096
CLASSES = 8
EXTRA_ROWS = 16


def butterfly_sum(x, axis, n):
    k = 1
    while k < n:
        perm = [(i, i ^ k) for i in range(n)]
        x = x + lax.ppermute(x, axis, perm)
        k *= 2
    return x


def body(activations, labels):
    tok_rows, slice_width = activations.shape
    n_dp = lax.axis_size("dp")
    assert n_dp & (n_dp - 1) == 0
    token_total = tok_rows * n_dp
    col_width = D // n_dp
    classes = jnp.arange(CLASSES, dtype=jnp.int32)
    matches = labels[None, :] == classes[:, None]
    onehot = matches.astype(jnp.bfloat16)
    local_counts = jnp.sum(matches.astype(jnp.float32), axis=1)
    own_local = jnp.dot(onehot, activations, preferred_element_type=jnp.float32)
    stats = jnp.concatenate(
        [own_local, jnp.broadcast_to(local_counts[:, None], (CLASSES, 128))], axis=1
    )

    n_t = lax.axis_size("tensor")
    assert n_t % 4 == 0 and n_dp == 2 * n_t and slice_width == 2 * col_width
    win = n_t // 4
    m = lax.axis_index("tensor")
    blocks = [None] * (2 * win + 1)
    blocks[win] = activations
    fwd = activations
    bwd = activations
    up = [(i, (i + 1) % n_t) for i in range(n_t)]
    down = [(i, (i - 1) % n_t) for i in range(n_t)]
    bfly = [1 << b for b in range(n_dp.bit_length() - 1)]
    per_step = [bfly[i::win] for i in range(win)]
    for step in range(1, win + 1):
        fwd = lax.ppermute(fwd, "tensor", up)
        bwd = lax.ppermute(bwd, "tensor", down)
        for k in per_step[step - 1]:
            stats = stats + lax.ppermute(stats, "dp", [(i, i ^ k) for i in range(n_dp)])
        fwd, bwd, stats = lax.optimization_barrier((fwd, bwd, stats))
        blocks[win - step] = fwd
        blocks[win + step] = bwd
    wst = jnp.stack(blocks)
    contract = (((1,), (0,)), ((), ()))
    near = lax.dot_general(wst, activations, contract, preferred_element_type=jnp.float32)
    far_a = lax.dot_general(
        wst[win + 1:], wst[0], contract, preferred_element_type=jnp.float32
    )
    n_b = n_t - 3 * win - 1
    far_b = lax.dot_general(
        wst[0], wst[win + 1:win + 1 + n_b], (((0,), (1,)), ((), ())),
        preferred_element_type=jnp.float32,
    ).transpose(1, 0, 2)
    prod = jnp.concatenate([near, far_a, far_b], axis=0).reshape(n_dp, col_width, slice_width)
    ones = jnp.ones((8, tok_rows), jnp.bfloat16)
    cs = lax.dot_general(wst, ones, (((1,), (1,)), ((), ())), preferred_element_type=jnp.float32)[..., 0]
    cs_off = jnp.concatenate([cs, cs[win + 1:], jnp.broadcast_to(cs[0], (n_b, slice_width))], axis=0)
    extra = jnp.pad(
        cs_off.reshape(n_dp, 1, col_width),
        ((0, 0), (0, EXTRA_ROWS - 1), (0, slice_width - col_width)),
    )
    off_payload = jnp.concatenate([prod, extra], axis=1)
    rows = col_width + EXTRA_ROWS
    half_rows = rows // 2
    shift = (2 * m - 2 * win) % n_dp
    doubled = jnp.concatenate([off_payload, off_payload], axis=0)
    payload = lax.dynamic_slice_in_dim(doubled, (n_dp - shift) % n_dp, n_dp, axis=0)

    me = lax.axis_index("dp")
    core = me & 1
    pairs = payload.reshape(n_dp // 2, 2, rows, slice_width)
    keep = lax.dynamic_index_in_dim(pairs, core, 1, keepdims=False)
    send = lax.dynamic_index_in_dim(pairs, 1 - core, 1, keepdims=False)
    core_swap = [(i, i ^ 1) for i in range(n_dp)]
    chip_sum = keep + lax.ppermute(send, "dp", core_swap)
    halves = chip_sum.reshape(n_dp, half_rows, slice_width)
    recv = lax.all_to_all(halves, "dp", 0, 0, tiled=True)
    by_core = jnp.sum(recv.reshape(n_dp // 2, 2, half_rows, slice_width), axis=0)
    mine = lax.dynamic_index_in_dim(by_core, core, 0, keepdims=False)
    other = lax.dynamic_index_in_dim(by_core, 1 - core, 0, keepdims=False)
    got = lax.ppermute(other, "dp", core_swap)
    total = jnp.where(
        core == 0, jnp.concatenate([mine, got], axis=0), jnp.concatenate([got, mine], axis=0)
    )
    me = lax.axis_index("dp")
    perm = []
    for src_s in range(n_dp):
        for src_m in range(n_t):
            o = (src_s // 2 - src_m) % n_t
            h = src_s % 2
            if win < o <= 2 * win:
                dst = ((src_s - 2 * win) % n_dp, (src_m - win) % n_t)
            elif o > 2 * win and o < n_t - win:
                dst = ((2 * (src_m - win) + h) % n_dp, (src_m + o - 2 * win) % n_t)
            else:
                continue
            perm.append((src_s * n_t + src_m, dst[0] * n_t + dst[1]))
    moved = lax.ppermute(total, ("dp", "tensor"), perm)
    my_o = (me // 2 - m) % n_t
    is_far = jnp.logical_and(my_o > win, my_o < n_t - win)
    final = jnp.where(is_far, moved, total)
    gram_cols = final[:col_width]
    mean_cols = final[col_width, :col_width] / token_total
    own_sums = stats[:, :slice_width]
    class_counts = stats[:, slice_width]
    mean_rows = jnp.sum(own_sums, axis=0) / token_total
    covariance = gram_cols.T / token_total - mean_rows[:, None] * mean_cols[None, :]
    cross_covariance = (own_sums - class_counts[:, None] * mean_rows[None, :]) / token_total
    return (covariance, cross_covariance)


def solution(mesh):
    in_specs = (P("dp", "tensor"), P("dp"))
    out_specs = (P("tensor", "dp"), P(None, "tensor"))
    return jax.shard_map(body, mesh=mesh, in_specs=in_specs, out_specs=out_specs, check_vma=False)
```

```python
import jax
import jax.numpy as jnp
from jax import lax
from jax.sharding import PartitionSpec as P

D = 4096
CLASSES = 8
EXTRA_ROWS = 16


def butterfly_sum(x, axis, n):
    k = 1
    while k < n:
        perm = [(i, i ^ k) for i in range(n)]
        x = x + lax.ppermute(x, axis, perm)
        k *= 2
    return x


def body(activations, labels):
    tok_rows, slice_width = activations.shape
    n_dp = lax.axis_size("dp")
    assert n_dp & (n_dp - 1) == 0
    token_total = tok_rows * n_dp
    col_width = D // n_dp
    classes = jnp.arange(CLASSES, dtype=jnp.int32)
    matches = labels[None, :] == classes[:, None]
    onehot = matches.astype(jnp.bfloat16)
    local_counts = jnp.sum(matches.astype(jnp.float32), axis=1)
    own_local = jnp.dot(onehot, activations, preferred_element_type=jnp.float32)
    stats = jnp.concatenate(
        [own_local, jnp.broadcast_to(local_counts[:, None], (CLASSES, 128))], axis=1
    )

    n_t = lax.axis_size("tensor")
    assert n_t % 4 == 0 and n_dp == 2 * n_t and slice_width == 2 * col_width
    win = n_t // 4
    m = lax.axis_index("tensor")
    blocks = [None] * (2 * win + 1)
    blocks[win] = activations
    fwd = activations
    bwd = activations
    up = [(i, (i + 1) % n_t) for i in range(n_t)]
    down = [(i, (i - 1) % n_t) for i in range(n_t)]
    bfly = [1 << b for b in range(n_dp.bit_length() - 1)]
    per_step = [bfly[i::win] for i in range(win)]
    contract = (((0,), (0,)), ((), ()))
    ones = jnp.ones((tok_rows, 8), jnp.bfloat16)

    def near_of(b):
        pr = lax.dot_general(b, activations, contract, preferred_element_type=jnp.float32)
        cs = lax.dot_general(b, ones, contract, preferred_element_type=jnp.float32)[:, 0]
        return pr, cs

    near = [None] * (2 * win + 1)
    colsums = [None] * (2 * win + 1)
    near[win], colsums[win] = near_of(activations)
    for step in range(1, win + 1):
        fwd = lax.ppermute(fwd, "tensor", up)
        bwd = lax.ppermute(bwd, "tensor", down)
        for k in per_step[step - 1]:
            stats = stats + lax.ppermute(stats, "dp", [(i, i ^ k) for i in range(n_dp)])
        ready = []
        if step > 1:
            for idx in (win - step + 1, win + step - 1):
                near[idx], colsums[idx] = near_of(blocks[idx])
                ready += [near[idx], colsums[idx]]
        fwd, bwd, stats, ready = lax.optimization_barrier((fwd, bwd, stats, ready))
        if step > 1:
            near[win - step + 1], colsums[win - step + 1] = ready[0], ready[1]
            near[win + step - 1], colsums[win + step - 1] = ready[2], ready[3]
        blocks[win - step] = fwd
        blocks[win + step] = bwd
    for idx in (0, 2 * win):
        near[idx], colsums[idx] = near_of(blocks[idx])
    n_b = n_t - 3 * win - 1
    far_a = [
        lax.dot_general(blocks[k], blocks[0], contract, preferred_element_type=jnp.float32)
        for k in range(win + 1, 2 * win + 1)
    ]
    far_b = [
        lax.dot_general(blocks[0], blocks[k], contract, preferred_element_type=jnp.float32)
        for k in range(win + 1, win + 1 + n_b)
    ]
    prod = jnp.stack(near + far_a + far_b).reshape(n_dp, col_width, slice_width)
    cs_off = jnp.stack(colsums + colsums[win + 1:] + [colsums[0]] * n_b)
    extra = jnp.pad(
        cs_off.reshape(n_dp, 1, col_width),
        ((0, 0), (0, EXTRA_ROWS - 1), (0, slice_width - col_width)),
    )
    off_payload = jnp.concatenate([prod, extra], axis=1)
    rows = col_width + EXTRA_ROWS
    half_rows = rows // 2
    shift = (2 * m - 2 * win) % n_dp
    doubled = jnp.concatenate([off_payload, off_payload], axis=0)
    payload = lax.dynamic_slice_in_dim(doubled, (n_dp - shift) % n_dp, n_dp, axis=0)

    me = lax.axis_index("dp")
    core = me & 1
    pairs = payload.reshape(n_dp // 2, 2, rows, slice_width)
    keep = lax.dynamic_index_in_dim(pairs, core, 1, keepdims=False)
    send = lax.dynamic_index_in_dim(pairs, 1 - core, 1, keepdims=False)
    core_swap = [(i, i ^ 1) for i in range(n_dp)]
    chip_sum = keep + lax.ppermute(send, "dp", core_swap)
    halves = chip_sum.reshape(n_dp, half_rows, slice_width)
    recv = lax.all_to_all(halves, "dp", 0, 0, tiled=True)
    by_core = jnp.sum(recv.reshape(n_dp // 2, 2, half_rows, slice_width), axis=0)
    mine = lax.dynamic_index_in_dim(by_core, core, 0, keepdims=False)
    other = lax.dynamic_index_in_dim(by_core, 1 - core, 0, keepdims=False)
    got = lax.ppermute(other, "dp", core_swap)
    total = jnp.where(
        core == 0, jnp.concatenate([mine, got], axis=0), jnp.concatenate([got, mine], axis=0)
    )
    me = lax.axis_index("dp")
    perm = []
    for src_s in range(n_dp):
        for src_m in range(n_t):
            o = (src_s // 2 - src_m) % n_t
            h = src_s % 2
            if win < o <= 2 * win:
                dst = ((src_s - 2 * win) % n_dp, (src_m - win) % n_t)
            elif o > 2 * win and o < n_t - win:
                dst = ((2 * (src_m - win) + h) % n_dp, (src_m + o - 2 * win) % n_t)
            else:
                continue
            perm.append((src_s * n_t + src_m, dst[0] * n_t + dst[1]))
    moved = lax.ppermute(total, ("dp", "tensor"), perm)
    my_o = (me // 2 - m) % n_t
    is_far = jnp.logical_and(my_o > win, my_o < n_t - win)
    final = jnp.where(is_far, moved, total)
    gram_cols = final[:col_width]
    mean_cols = final[col_width, :col_width] / token_total
    own_sums = stats[:, :slice_width]
    class_counts = stats[:, slice_width]
    mean_rows = jnp.sum(own_sums, axis=0) / token_total
    covariance = gram_cols.T / token_total - mean_rows[:, None] * mean_cols[None, :]
    cross_covariance = (own_sums - class_counts[:, None] * mean_rows[None, :]) / token_total
    return (covariance, cross_covariance)


def solution(mesh):
    in_specs = (P("dp", "tensor"), P("dp"))
    out_specs = (P("tensor", "dp"), P(None, "tensor"))
    return jax.shard_map(body, mesh=mesh, in_specs=in_specs, out_specs=out_specs, check_vma=False)
```

```python
import jax
import jax.numpy as jnp
from jax import lax
from jax.sharding import PartitionSpec as P

D = 4096
CLASSES = 8
EXTRA_ROWS = 16


def butterfly_sum(x, axis, n):
    k = 1
    while k < n:
        perm = [(i, i ^ k) for i in range(n)]
        x = x + lax.ppermute(x, axis, perm)
        k *= 2
    return x


def body(activations, labels):
    tok_rows, slice_width = activations.shape
    n_dp = lax.axis_size("dp")
    assert n_dp & (n_dp - 1) == 0
    token_total = tok_rows * n_dp
    col_width = D // n_dp
    classes = jnp.arange(CLASSES, dtype=jnp.int32)
    matches = labels[None, :] == classes[:, None]
    onehot = matches.astype(jnp.bfloat16)
    local_counts = jnp.sum(matches.astype(jnp.float32), axis=1)
    own_local = jnp.dot(onehot, activations, preferred_element_type=jnp.float32)
    stats = jnp.concatenate(
        [own_local, jnp.broadcast_to(local_counts[:, None], (CLASSES, 128))], axis=1
    )

    n_t = lax.axis_size("tensor")
    assert n_t % 4 == 0 and n_dp == 2 * n_t and slice_width == 2 * col_width
    win = n_t // 4
    m = lax.axis_index("tensor")
    blocks = [None] * (2 * win + 1)
    blocks[win] = activations
    fwd = activations
    bwd = activations
    up = [(i, (i + 1) % n_t) for i in range(n_t)]
    down = [(i, (i - 1) % n_t) for i in range(n_t)]
    bfly = [1 << b for b in range(n_dp.bit_length() - 1)]
    per_step = [bfly[i::win] for i in range(win)]
    for step in range(1, win + 1):
        fwd = lax.ppermute(fwd, "tensor", up)
        bwd = lax.ppermute(bwd, "tensor", down)
        for k in per_step[step - 1]:
            stats = stats + lax.ppermute(stats, "dp", [(i, i ^ k) for i in range(n_dp)])
        fwd, bwd, stats = lax.optimization_barrier((fwd, bwd, stats))
        blocks[win - step] = fwd
        blocks[win + step] = bwd
    wst = jnp.stack(blocks)
    contract = (((1,), (0,)), ((), ()))
    near = lax.dot_general(wst, activations, contract, preferred_element_type=jnp.float32)
    far_a = lax.dot_general(
        wst[win + 1:], wst[0], contract, preferred_element_type=jnp.float32
    )
    n_b = n_t - 3 * win - 1
    far_b = lax.dot_general(
        wst[0], wst[win + 1:win + 1 + n_b], (((0,), (1,)), ((), ())),
        preferred_element_type=jnp.float32,
    ).transpose(1, 0, 2)
    prod = jnp.concatenate([near, far_a, far_b], axis=0)
    ones = jnp.ones((8, tok_rows), jnp.bfloat16)
    cs = lax.dot_general(wst, ones, (((1,), (1,)), ((), ())), preferred_element_type=jnp.float32)[..., 0]
    cs_off = jnp.concatenate([cs, cs[win + 1:], jnp.broadcast_to(cs[0], (n_b, slice_width))], axis=0)
    rows = col_width + EXTRA_ROWS
    half_rows = rows // 2

    me = lax.axis_index("dp")
    core = me & 1
    p2 = prod.reshape(n_t, 2, col_width, slice_width)
    c2 = cs_off.reshape(n_t, 2, 1, col_width)

    def half(h):
        extra = jnp.pad(
            lax.dynamic_index_in_dim(c2, h, 1, keepdims=False),
            ((0, 0), (0, EXTRA_ROWS - 1), (0, slice_width - col_width)),
        )
        return jnp.concatenate([lax.dynamic_index_in_dim(p2, h, 1, keepdims=False), extra], axis=1)

    core_swap = [(i, i ^ 1) for i in range(n_dp)]
    summed = half(core) + lax.ppermute(half(1 - core), "dp", core_swap)
    shift = (m - win) % n_t
    doubled = jnp.concatenate([summed, summed], axis=0)
    chip_sum = lax.dynamic_slice_in_dim(doubled, (n_t - shift) % n_t, n_t, axis=0)
    halves = chip_sum.reshape(n_dp, half_rows, slice_width)
    recv = lax.all_to_all(halves, "dp", 0, 0, tiled=True)
    by_core = jnp.sum(recv.reshape(n_dp // 2, 2, half_rows, slice_width), axis=0)
    mine = lax.dynamic_index_in_dim(by_core, core, 0, keepdims=False)
    other = lax.dynamic_index_in_dim(by_core, 1 - core, 0, keepdims=False)
    got = lax.ppermute(other, "dp", core_swap)
    total = jnp.where(
        core == 0, jnp.concatenate([mine, got], axis=0), jnp.concatenate([got, mine], axis=0)
    )
    me = lax.axis_index("dp")
    perm = []
    for src_s in range(n_dp):
        for src_m in range(n_t):
            o = (src_s // 2 - src_m) % n_t
            h = src_s % 2
            if win < o <= 2 * win:
                dst = ((src_s - 2 * win) % n_dp, (src_m - win) % n_t)
            elif o > 2 * win and o < n_t - win:
                dst = ((2 * (src_m - win) + h) % n_dp, (src_m + o - 2 * win) % n_t)
            else:
                continue
            perm.append((src_s * n_t + src_m, dst[0] * n_t + dst[1]))
    moved = lax.ppermute(total, ("dp", "tensor"), perm)
    my_o = (me // 2 - m) % n_t
    is_far = jnp.logical_and(my_o > win, my_o < n_t - win)
    final = jnp.where(is_far, moved, total)
    gram_cols = final[:col_width]
    mean_cols = final[col_width, :col_width] / token_total
    own_sums = stats[:, :slice_width]
    class_counts = stats[:, slice_width]
    mean_rows = jnp.sum(own_sums, axis=0) / token_total
    covariance = gram_cols.T / token_total - mean_rows[:, None] * mean_cols[None, :]
    cross_covariance = (own_sums - class_counts[:, None] * mean_rows[None, :]) / token_total
    return (covariance, cross_covariance)


def solution(mesh):
    in_specs = (P("dp", "tensor"), P("dp"))
    out_specs = (P("tensor", "dp"), P(None, "tensor"))
    return jax.shard_map(body, mesh=mesh, in_specs=in_specs, out_specs=out_specs, check_vma=False)
```

```python
import jax
import jax.numpy as jnp
from jax import lax
from jax.sharding import PartitionSpec as P

D = 4096
CLASSES = 8
EXTRA_ROWS = 16


def butterfly_sum(x, axis, n):
    k = 1
    while k < n:
        perm = [(i, i ^ k) for i in range(n)]
        x = x + lax.ppermute(x, axis, perm)
        k *= 2
    return x


def body(activations, labels):
    tok_rows, slice_width = activations.shape
    n_dp = lax.axis_size("dp")
    assert n_dp & (n_dp - 1) == 0
    token_total = tok_rows * n_dp
    col_width = D // n_dp
    classes = jnp.arange(CLASSES, dtype=jnp.int32)
    matches = labels[None, :] == classes[:, None]
    onehot = matches.astype(jnp.bfloat16)
    local_counts = jnp.sum(matches.astype(jnp.float32), axis=1)
    own_local = jnp.dot(onehot, activations, preferred_element_type=jnp.float32)
    stats = jnp.concatenate(
        [own_local, jnp.broadcast_to(local_counts[:, None], (CLASSES, 128))], axis=1
    )

    n_t = lax.axis_size("tensor")
    assert n_t % 4 == 0 and n_dp == 2 * n_t and slice_width == 2 * col_width
    win = n_t // 4
    m = lax.axis_index("tensor")
    blocks = [None] * (2 * win + 1)
    blocks[win] = activations
    fwd = activations
    bwd = activations
    up = [(i, (i + 1) % n_t) for i in range(n_t)]
    down = [(i, (i - 1) % n_t) for i in range(n_t)]
    stats = lax.psum(jnp.pad(stats, ((0, 0), (0, D - stats.shape[1]))), "dp")
    for step in range(1, win + 1):
        fwd = lax.ppermute(fwd, "tensor", up)
        bwd = lax.ppermute(bwd, "tensor", down)
        fwd, bwd = lax.optimization_barrier((fwd, bwd))
        blocks[win - step] = fwd
        blocks[win + step] = bwd
    wst = jnp.stack(blocks)
    wst, stats = lax.optimization_barrier((wst, stats))
    contract = (((1,), (0,)), ((), ()))
    near = lax.dot_general(wst, activations, contract, preferred_element_type=jnp.float32)
    far_a = lax.dot_general(
        wst[win + 1:], wst[0], contract, preferred_element_type=jnp.float32
    )
    n_b = n_t - 3 * win - 1
    far_b = lax.dot_general(
        wst[0], wst[win + 1:win + 1 + n_b], (((0,), (1,)), ((), ())),
        preferred_element_type=jnp.float32,
    ).transpose(1, 0, 2)
    prod = jnp.concatenate([near, far_a, far_b], axis=0)
    ones = jnp.ones((8, tok_rows), jnp.bfloat16)
    cs = lax.dot_general(wst, ones, (((1,), (1,)), ((), ())), preferred_element_type=jnp.float32)[..., 0]
    cs_off = jnp.concatenate([cs, cs[win + 1:], jnp.broadcast_to(cs[0], (n_b, slice_width))], axis=0)
    rows = col_width + EXTRA_ROWS
    half_rows = rows // 2

    me = lax.axis_index("dp")
    core = me & 1
    p2 = prod.reshape(n_t, 2, col_width, slice_width)
    c2 = cs_off.reshape(n_t, 2, 1, col_width)

    def half(h):
        extra = jnp.pad(
            lax.dynamic_index_in_dim(c2, h, 1, keepdims=False),
            ((0, 0), (0, EXTRA_ROWS - 1), (0, slice_width - col_width)),
        )
        return jnp.concatenate([lax.dynamic_index_in_dim(p2, h, 1, keepdims=False), extra], axis=1)

    core_swap = [(i, i ^ 1) for i in range(n_dp)]
    summed = half(core) + lax.ppermute(half(1 - core), "dp", core_swap)
    shift = (m - win) % n_t
    doubled = jnp.concatenate([summed, summed], axis=0)
    chip_sum = lax.dynamic_slice_in_dim(doubled, (n_t - shift) % n_t, n_t, axis=0)
    halves = chip_sum.reshape(n_dp, half_rows, slice_width)
    recv = lax.all_to_all(halves, "dp", 0, 0, tiled=True)
    by_core = jnp.sum(recv.reshape(n_dp // 2, 2, half_rows, slice_width), axis=0)
    mine = lax.dynamic_index_in_dim(by_core, core, 0, keepdims=False)
    other = lax.dynamic_index_in_dim(by_core, 1 - core, 0, keepdims=False)
    got = lax.ppermute(other, "dp", core_swap)
    total = jnp.where(
        core == 0, jnp.concatenate([mine, got], axis=0), jnp.concatenate([got, mine], axis=0)
    )
    me = lax.axis_index("dp")
    perm = []
    for src_s in range(n_dp):
        for src_m in range(n_t):
            o = (src_s // 2 - src_m) % n_t
            h = src_s % 2
            if win < o <= 2 * win:
                dst = ((src_s - 2 * win) % n_dp, (src_m - win) % n_t)
            elif o > 2 * win and o < n_t - win:
                dst = ((2 * (src_m - win) + h) % n_dp, (src_m + o - 2 * win) % n_t)
            else:
                continue
            perm.append((src_s * n_t + src_m, dst[0] * n_t + dst[1]))
    moved = lax.ppermute(total, ("dp", "tensor"), perm)
    my_o = (me // 2 - m) % n_t
    is_far = jnp.logical_and(my_o > win, my_o < n_t - win)
    final = jnp.where(is_far, moved, total)
    gram_cols = final[:col_width]
    mean_cols = final[col_width, :col_width] / token_total
    own_sums = stats[:, :slice_width]
    class_counts = stats[:, slice_width]
    mean_rows = jnp.sum(own_sums, axis=0) / token_total
    covariance = gram_cols.T / token_total - mean_rows[:, None] * mean_cols[None, :]
    cross_covariance = (own_sums - class_counts[:, None] * mean_rows[None, :]) / token_total
    return (covariance, cross_covariance)


def solution(mesh):
    in_specs = (P("dp", "tensor"), P("dp"))
    out_specs = (P("tensor", "dp"), P(None, "tensor"))
    return jax.shard_map(body, mesh=mesh, in_specs=in_specs, out_specs=out_specs, check_vma=False)
```

```python
import jax
import jax.numpy as jnp
from jax import lax
from jax.sharding import PartitionSpec as P

D = 4096
CLASSES = 8
EXTRA_ROWS = 16


def butterfly_sum(x, axis, n):
    k = 1
    while k < n:
        perm = [(i, i ^ k) for i in range(n)]
        x = x + lax.ppermute(x, axis, perm)
        k *= 2
    return x


def body(activations, labels):
    tok_rows, slice_width = activations.shape
    n_dp = lax.axis_size("dp")
    assert n_dp & (n_dp - 1) == 0
    token_total = tok_rows * n_dp
    col_width = D // n_dp
    classes = jnp.arange(CLASSES, dtype=jnp.int32)
    matches = labels[None, :] == classes[:, None]
    onehot = matches.astype(jnp.bfloat16)
    local_counts = jnp.sum(matches.astype(jnp.float32), axis=1)
    own_local = jnp.dot(onehot, activations, preferred_element_type=jnp.float32)
    stats = jnp.concatenate(
        [own_local, jnp.broadcast_to(local_counts[:, None], (CLASSES, 128))], axis=1
    )

    n_t = lax.axis_size("tensor")
    assert n_t % 4 == 0 and n_dp == 2 * n_t and slice_width == 2 * col_width
    win = n_t // 4
    m = lax.axis_index("tensor")
    blocks = [None] * (2 * win + 1)
    blocks[win] = activations
    fwd = activations
    bwd = activations
    up = [(i, (i + 1) % n_t) for i in range(n_t)]
    down = [(i, (i - 1) % n_t) for i in range(n_t)]
    for step in range(1, win + 1):
        fwd = lax.ppermute(fwd, "tensor", up)
        bwd = lax.ppermute(bwd, "tensor", down)
        if step == 1:
            rep = jnp.broadcast_to(stats[None], (n_dp,) + stats.shape)
            stats = jnp.sum(lax.all_to_all(rep, "dp", 0, 0, tiled=True), axis=0)
        fwd, bwd, stats = lax.optimization_barrier((fwd, bwd, stats))
        blocks[win - step] = fwd
        blocks[win + step] = bwd
    wst = jnp.stack(blocks)
    contract = (((1,), (0,)), ((), ()))
    near = lax.dot_general(wst, activations, contract, preferred_element_type=jnp.float32)
    far_a = lax.dot_general(
        wst[win + 1:], wst[0], contract, preferred_element_type=jnp.float32
    )
    n_b = n_t - 3 * win - 1
    far_b = lax.dot_general(
        wst[0], wst[win + 1:win + 1 + n_b], (((0,), (1,)), ((), ())),
        preferred_element_type=jnp.float32,
    ).transpose(1, 0, 2)
    prod = jnp.concatenate([near, far_a, far_b], axis=0)
    ones = jnp.ones((8, tok_rows), jnp.bfloat16)
    cs = lax.dot_general(wst, ones, (((1,), (1,)), ((), ())), preferred_element_type=jnp.float32)[..., 0]
    cs_off = jnp.concatenate([cs, cs[win + 1:], jnp.broadcast_to(cs[0], (n_b, slice_width))], axis=0)
    rows = col_width + EXTRA_ROWS
    half_rows = rows // 2

    me = lax.axis_index("dp")
    core = me & 1
    p2 = prod.reshape(n_t, 2, col_width, slice_width)
    c2 = cs_off.reshape(n_t, 2, 1, col_width)

    def half(h):
        extra = jnp.pad(
            lax.dynamic_index_in_dim(c2, h, 1, keepdims=False),
            ((0, 0), (0, EXTRA_ROWS - 1), (0, slice_width - col_width)),
        )
        return jnp.concatenate([lax.dynamic_index_in_dim(p2, h, 1, keepdims=False), extra], axis=1)

    core_swap = [(i, i ^ 1) for i in range(n_dp)]
    summed = half(core) + lax.ppermute(half(1 - core), "dp", core_swap)
    shift = (m - win) % n_t
    doubled = jnp.concatenate([summed, summed], axis=0)
    chip_sum = lax.dynamic_slice_in_dim(doubled, (n_t - shift) % n_t, n_t, axis=0)
    halves = chip_sum.reshape(n_dp, half_rows, slice_width)
    recv = lax.all_to_all(halves, "dp", 0, 0, tiled=True)
    by_core = jnp.sum(recv.reshape(n_dp // 2, 2, half_rows, slice_width), axis=0)
    mine = lax.dynamic_index_in_dim(by_core, core, 0, keepdims=False)
    other = lax.dynamic_index_in_dim(by_core, 1 - core, 0, keepdims=False)
    got = lax.ppermute(other, "dp", core_swap)
    total = jnp.where(
        core == 0, jnp.concatenate([mine, got], axis=0), jnp.concatenate([got, mine], axis=0)
    )
    me = lax.axis_index("dp")
    perm = []
    for src_s in range(n_dp):
        for src_m in range(n_t):
            o = (src_s // 2 - src_m) % n_t
            h = src_s % 2
            if win < o <= 2 * win:
                dst = ((src_s - 2 * win) % n_dp, (src_m - win) % n_t)
            elif o > 2 * win and o < n_t - win:
                dst = ((2 * (src_m - win) + h) % n_dp, (src_m + o - 2 * win) % n_t)
            else:
                continue
            perm.append((src_s * n_t + src_m, dst[0] * n_t + dst[1]))
    moved = lax.ppermute(total, ("dp", "tensor"), perm)
    my_o = (me // 2 - m) % n_t
    is_far = jnp.logical_and(my_o > win, my_o < n_t - win)
    final = jnp.where(is_far, moved, total)
    gram_cols = final[:col_width]
    mean_cols = final[col_width, :col_width] / token_total
    own_sums = stats[:, :slice_width]
    class_counts = stats[:, slice_width]
    mean_rows = jnp.sum(own_sums, axis=0) / token_total
    covariance = gram_cols.T / token_total - mean_rows[:, None] * mean_cols[None, :]
    cross_covariance = (own_sums - class_counts[:, None] * mean_rows[None, :]) / token_total
    return (covariance, cross_covariance)


def solution(mesh):
    in_specs = (P("dp", "tensor"), P("dp"))
    out_specs = (P("tensor", "dp"), P(None, "tensor"))
    return jax.shard_map(body, mesh=mesh, in_specs=in_specs, out_specs=out_specs, check_vma=False)
```

```python
import jax
import jax.numpy as jnp
from jax import lax
from jax.sharding import PartitionSpec as P

D = 4096
CLASSES = 8
EXTRA_ROWS = 16


def butterfly_sum(x, axis, n):
    k = 1
    while k < n:
        perm = [(i, i ^ k) for i in range(n)]
        x = x + lax.ppermute(x, axis, perm)
        k *= 2
    return x


def body(activations, labels):
    tok_rows, slice_width = activations.shape
    n_dp = lax.axis_size("dp")
    assert n_dp & (n_dp - 1) == 0
    token_total = tok_rows * n_dp
    col_width = D // n_dp
    classes = jnp.arange(CLASSES, dtype=jnp.int32)
    matches = labels[None, :] == classes[:, None]
    onehot = matches.astype(jnp.bfloat16)
    local_counts = jnp.sum(matches.astype(jnp.float32), axis=1)
    own_local = jnp.dot(onehot, activations, preferred_element_type=jnp.float32)
    stats = jnp.concatenate(
        [own_local, jnp.broadcast_to(local_counts[:, None], (CLASSES, 128))], axis=1
    )

    n_t = lax.axis_size("tensor")
    assert n_t % 4 == 0 and n_dp == 2 * n_t and slice_width == 2 * col_width
    win = n_t // 4
    m = lax.axis_index("tensor")
    blocks = [None] * (2 * win + 1)
    blocks[win] = activations
    fwd = activations
    bwd = activations
    up = [(i, (i + 1) % n_t) for i in range(n_t)]
    down = [(i, (i - 1) % n_t) for i in range(n_t)]
    bfly = [1 << b for b in range(n_dp.bit_length() - 1)]
    per_step = [[k] for k in bfly[:win]]
    late_bfly = bfly[win:]
    for step in range(1, win + 1):
        fwd = lax.ppermute(fwd, "tensor", up)
        bwd = lax.ppermute(bwd, "tensor", down)
        for k in per_step[step - 1]:
            stats = stats + lax.ppermute(stats, "dp", [(i, i ^ k) for i in range(n_dp)])
        fwd, bwd, stats = lax.optimization_barrier((fwd, bwd, stats))
        blocks[win - step] = fwd
        blocks[win + step] = bwd
    wst = jnp.stack(blocks)
    contract = (((1,), (0,)), ((), ()))
    near = lax.dot_general(wst, activations, contract, preferred_element_type=jnp.float32)
    far_a = lax.dot_general(
        wst[win + 1:], wst[0], contract, preferred_element_type=jnp.float32
    )
    n_b = n_t - 3 * win - 1
    far_b = lax.dot_general(
        wst[0], wst[win + 1:win + 1 + n_b], (((0,), (1,)), ((), ())),
        preferred_element_type=jnp.float32,
    ).transpose(1, 0, 2)
    prod = jnp.concatenate([near, far_a, far_b], axis=0)
    ones = jnp.ones((8, tok_rows), jnp.bfloat16)
    cs = lax.dot_general(wst, ones, (((1,), (1,)), ((), ())), preferred_element_type=jnp.float32)[..., 0]
    cs_off = jnp.concatenate([cs, cs[win + 1:], jnp.broadcast_to(cs[0], (n_b, slice_width))], axis=0)
    rows = col_width + EXTRA_ROWS
    half_rows = rows // 2

    me = lax.axis_index("dp")
    core = me & 1
    p2 = prod.reshape(n_t, 2, col_width, slice_width)
    c2 = cs_off.reshape(n_t, 2, 1, col_width)

    def half(h):
        extra = jnp.pad(
            lax.dynamic_index_in_dim(c2, h, 1, keepdims=False),
            ((0, 0), (0, EXTRA_ROWS - 1), (0, slice_width - col_width)),
        )
        return jnp.concatenate([lax.dynamic_index_in_dim(p2, h, 1, keepdims=False), extra], axis=1)

    core_swap = [(i, i ^ 1) for i in range(n_dp)]
    swapped = lax.ppermute(half(1 - core), "dp", core_swap)
    for k in late_bfly:
        stats = stats + lax.ppermute(stats, "dp", [(i, i ^ k) for i in range(n_dp)])
    swapped, stats = lax.optimization_barrier((swapped, stats))
    summed = half(core) + swapped
    shift = (m - win) % n_t
    doubled = jnp.concatenate([summed, summed], axis=0)
    chip_sum = lax.dynamic_slice_in_dim(doubled, (n_t - shift) % n_t, n_t, axis=0)
    halves = chip_sum.reshape(n_dp, half_rows, slice_width)
    recv = lax.all_to_all(halves, "dp", 0, 0, tiled=True)
    by_core = jnp.sum(recv.reshape(n_dp // 2, 2, half_rows, slice_width), axis=0)
    mine = lax.dynamic_index_in_dim(by_core, core, 0, keepdims=False)
    other = lax.dynamic_index_in_dim(by_core, 1 - core, 0, keepdims=False)
    got = lax.ppermute(other, "dp", core_swap)
    total = jnp.where(
        core == 0, jnp.concatenate([mine, got], axis=0), jnp.concatenate([got, mine], axis=0)
    )
    me = lax.axis_index("dp")
    perm = []
    for src_s in range(n_dp):
        for src_m in range(n_t):
            o = (src_s // 2 - src_m) % n_t
            h = src_s % 2
            if win < o <= 2 * win:
                dst = ((src_s - 2 * win) % n_dp, (src_m - win) % n_t)
            elif o > 2 * win and o < n_t - win:
                dst = ((2 * (src_m - win) + h) % n_dp, (src_m + o - 2 * win) % n_t)
            else:
                continue
            perm.append((src_s * n_t + src_m, dst[0] * n_t + dst[1]))
    moved = lax.ppermute(total, ("dp", "tensor"), perm)
    my_o = (me // 2 - m) % n_t
    is_far = jnp.logical_and(my_o > win, my_o < n_t - win)
    final = jnp.where(is_far, moved, total)
    gram_cols = final[:col_width]
    mean_cols = final[col_width, :col_width] / token_total
    own_sums = stats[:, :slice_width]
    class_counts = stats[:, slice_width]
    mean_rows = jnp.sum(own_sums, axis=0) / token_total
    covariance = gram_cols.T / token_total - mean_rows[:, None] * mean_cols[None, :]
    cross_covariance = (own_sums - class_counts[:, None] * mean_rows[None, :]) / token_total
    return (covariance, cross_covariance)


def solution(mesh):
    in_specs = (P("dp", "tensor"), P("dp"))
    out_specs = (P("tensor", "dp"), P(None, "tensor"))
    return jax.shard_map(body, mesh=mesh, in_specs=in_specs, out_specs=out_specs, check_vma=False)
```

```python
import jax
import jax.numpy as jnp
from jax import lax
from jax.sharding import PartitionSpec as P

D = 4096
CLASSES = 8
EXTRA_ROWS = 16


def butterfly_sum(x, axis, n):
    k = 1
    while k < n:
        perm = [(i, i ^ k) for i in range(n)]
        x = x + lax.ppermute(x, axis, perm)
        k *= 2
    return x


def body(activations, labels):
    tok_rows, slice_width = activations.shape
    n_dp = lax.axis_size("dp")
    assert n_dp & (n_dp - 1) == 0
    token_total = tok_rows * n_dp
    col_width = D // n_dp
    classes = jnp.arange(CLASSES, dtype=jnp.int32)
    matches = labels[None, :] == classes[:, None]
    onehot = matches.astype(jnp.bfloat16)
    local_counts = jnp.sum(matches.astype(jnp.float32), axis=1)
    own_local = jnp.dot(onehot, activations, preferred_element_type=jnp.float32)
    stats = jnp.concatenate(
        [own_local, jnp.broadcast_to(local_counts[:, None], (CLASSES, 128))], axis=1
    )

    n_t = lax.axis_size("tensor")
    assert n_t % 4 == 0 and n_dp == 2 * n_t and slice_width == 2 * col_width
    win = n_t // 4
    m = lax.axis_index("tensor")
    blocks = [None] * (2 * win + 1)
    blocks[win] = activations
    fwd = activations
    bwd = activations
    up = [(i, (i + 1) % n_t) for i in range(n_t)]
    down = [(i, (i - 1) % n_t) for i in range(n_t)]
    bfly = [1 << b for b in range(n_dp.bit_length() - 1)]
    per_step = [bfly[:1], bfly[1:2] + bfly[win:], bfly[2:3], bfly[3:win]]
    for step in range(1, win + 1):
        fwd = lax.ppermute(fwd, "tensor", up)
        bwd = lax.ppermute(bwd, "tensor", down)
        for k in per_step[step - 1]:
            stats = stats + lax.ppermute(stats, "dp", [(i, i ^ k) for i in range(n_dp)])
        fwd, bwd, stats = lax.optimization_barrier((fwd, bwd, stats))
        blocks[win - step] = fwd
        blocks[win + step] = bwd
    wst = jnp.stack(blocks)
    contract = (((1,), (0,)), ((), ()))
    near = lax.dot_general(wst, activations, contract, preferred_element_type=jnp.float32)
    far_a = lax.dot_general(
        wst[win + 1:], wst[0], contract, preferred_element_type=jnp.float32
    )
    n_b = n_t - 3 * win - 1
    far_b = lax.dot_general(
        wst[0], wst[win + 1:win + 1 + n_b], (((0,), (1,)), ((), ())),
        preferred_element_type=jnp.float32,
    ).transpose(1, 0, 2)
    prod = jnp.concatenate([near, far_a, far_b], axis=0)
    ones = jnp.ones((8, tok_rows), jnp.bfloat16)
    cs = lax.dot_general(wst, ones, (((1,), (1,)), ((), ())), preferred_element_type=jnp.float32)[..., 0]
    cs_off = jnp.concatenate([cs, cs[win + 1:], jnp.broadcast_to(cs[0], (n_b, slice_width))], axis=0)
    rows = col_width + EXTRA_ROWS
    half_rows = rows // 2

    me = lax.axis_index("dp")
    core = me & 1
    p2 = prod.reshape(n_t, 2, col_width, slice_width)
    c2 = cs_off.reshape(n_t, 2, 1, col_width)

    def half(h):
        extra = jnp.pad(
            lax.dynamic_index_in_dim(c2, h, 1, keepdims=False),
            ((0, 0), (0, EXTRA_ROWS - 1), (0, slice_width - col_width)),
        )
        return jnp.concatenate([lax.dynamic_index_in_dim(p2, h, 1, keepdims=False), extra], axis=1)

    core_swap = [(i, i ^ 1) for i in range(n_dp)]
    summed = half(core) + lax.ppermute(half(1 - core), "dp", core_swap)
    shift = (m - win) % n_t
    doubled = jnp.concatenate([summed, summed], axis=0)
    chip_sum = lax.dynamic_slice_in_dim(doubled, (n_t - shift) % n_t, n_t, axis=0)
    halves = chip_sum.reshape(n_dp, half_rows, slice_width)
    recv = lax.all_to_all(halves, "dp", 0, 0, tiled=True)
    by_core = jnp.sum(recv.reshape(n_dp // 2, 2, half_rows, slice_width), axis=0)
    mine = lax.dynamic_index_in_dim(by_core, core, 0, keepdims=False)
    other = lax.dynamic_index_in_dim(by_core, 1 - core, 0, keepdims=False)
    got = lax.ppermute(other, "dp", core_swap)
    total = jnp.where(
        core == 0, jnp.concatenate([mine, got], axis=0), jnp.concatenate([got, mine], axis=0)
    )
    me = lax.axis_index("dp")
    perm = []
    for src_s in range(n_dp):
        for src_m in range(n_t):
            o = (src_s // 2 - src_m) % n_t
            h = src_s % 2
            if win < o <= 2 * win:
                dst = ((src_s - 2 * win) % n_dp, (src_m - win) % n_t)
            elif o > 2 * win and o < n_t - win:
                dst = ((2 * (src_m - win) + h) % n_dp, (src_m + o - 2 * win) % n_t)
            else:
                continue
            perm.append((src_s * n_t + src_m, dst[0] * n_t + dst[1]))
    moved = lax.ppermute(total, ("dp", "tensor"), perm)
    my_o = (me // 2 - m) % n_t
    is_far = jnp.logical_and(my_o > win, my_o < n_t - win)
    final = jnp.where(is_far, moved, total)
    gram_cols = final[:col_width]
    mean_cols = final[col_width, :col_width] / token_total
    own_sums = stats[:, :slice_width]
    class_counts = stats[:, slice_width]
    mean_rows = jnp.sum(own_sums, axis=0) / token_total
    covariance = gram_cols.T / token_total - mean_rows[:, None] * mean_cols[None, :]
    cross_covariance = (own_sums - class_counts[:, None] * mean_rows[None, :]) / token_total
    return (covariance, cross_covariance)


def solution(mesh):
    in_specs = (P("dp", "tensor"), P("dp"))
    out_specs = (P("tensor", "dp"), P(None, "tensor"))
    return jax.shard_map(body, mesh=mesh, in_specs=in_specs, out_specs=out_specs, check_vma=False)
```

```python
import jax
import jax.numpy as jnp
from jax import lax
from jax.sharding import PartitionSpec as P

D = 4096
CLASSES = 8
EXTRA_ROWS = 16


def butterfly_sum(x, axis, n):
    k = 1
    while k < n:
        perm = [(i, i ^ k) for i in range(n)]
        x = x + lax.ppermute(x, axis, perm)
        k *= 2
    return x


def body(activations, labels):
    tok_rows, slice_width = activations.shape
    n_dp = lax.axis_size("dp")
    assert n_dp & (n_dp - 1) == 0
    token_total = tok_rows * n_dp
    col_width = D // n_dp
    classes = jnp.arange(CLASSES, dtype=jnp.int32)
    matches = labels[None, :] == classes[:, None]
    onehot = matches.astype(jnp.bfloat16)
    local_counts = jnp.sum(matches.astype(jnp.float32), axis=1)
    own_local = jnp.dot(onehot, activations, preferred_element_type=jnp.float32)
    stats = jnp.concatenate(
        [own_local, jnp.broadcast_to(local_counts[:, None], (CLASSES, 128))], axis=1
    )

    n_t = lax.axis_size("tensor")
    assert n_t % 4 == 0 and n_dp == 2 * n_t and slice_width == 2 * col_width
    win = n_t // 4
    m = lax.axis_index("tensor")
    blocks = [None] * (2 * win + 1)
    blocks[win] = activations
    fwd = activations
    bwd = activations
    up = [(i, (i + 1) % n_t) for i in range(n_t)]
    down = [(i, (i - 1) % n_t) for i in range(n_t)]
    bfly = [1 << b for b in range(n_dp.bit_length() - 1)]
    per_step = [bfly[i::win] for i in range(win)]
    for step in range(1, win + 1):
        fwd = lax.ppermute(fwd, "tensor", up)
        bwd = lax.ppermute(bwd, "tensor", down)
        for k in per_step[step - 1]:
            stats = stats + lax.ppermute(stats, "dp", [(i, i ^ k) for i in range(n_dp)])
        fwd, bwd, stats = lax.optimization_barrier((fwd, bwd, stats))
        blocks[win - step] = fwd
        blocks[win + step] = bwd
    wst = jnp.stack(blocks)
    contract = (((1,), (0,)), ((), ()))
    near = lax.dot_general(wst, activations, contract, preferred_element_type=jnp.float32)
    far_a = lax.dot_general(
        wst[win + 1:], wst[0], contract, preferred_element_type=jnp.float32
    )
    n_b = n_t - 3 * win - 1
    far_b = lax.dot_general(
        wst[0], wst[win + 1:win + 1 + n_b], (((0,), (1,)), ((), ())),
        preferred_element_type=jnp.float32,
    ).transpose(1, 0, 2)
    prod = jnp.concatenate([near, far_a, far_b], axis=0)
    ones = jnp.ones((8, tok_rows), jnp.bfloat16)
    cs = lax.dot_general(wst, ones, (((1,), (1,)), ((), ())), preferred_element_type=jnp.float32)[..., 0]
    cs_off = jnp.concatenate([cs, cs[win + 1:], jnp.broadcast_to(cs[0], (n_b, slice_width))], axis=0)
    rows = col_width + EXTRA_ROWS
    half_rows = rows // 2

    me = lax.axis_index("dp")
    core = me & 1
    p2 = prod.reshape(n_t, 2, col_width, slice_width)
    c2 = cs_off.reshape(n_t, 2, 1, col_width)

    def half(h):
        extra = jnp.pad(
            lax.dynamic_index_in_dim(c2, h, 1, keepdims=False),
            ((0, 0), (0, EXTRA_ROWS - 1), (0, slice_width - col_width)),
        )
        return jnp.concatenate([lax.dynamic_index_in_dim(p2, h, 1, keepdims=False), extra], axis=1)

    core_swap = [(i, i ^ 1) for i in range(n_dp)]
    summed = half(core) + lax.ppermute(half(1 - core), "dp", core_swap)
    shift = (m - win) % n_t
    doubled = jnp.concatenate([summed, summed], axis=0)
    chip_sum = lax.dynamic_slice_in_dim(doubled, (n_t - shift) % n_t, n_t, axis=0)
    halves = chip_sum.reshape(n_dp, half_rows, slice_width)
    recv = lax.all_to_all(halves, "dp", 0, 0, tiled=True)
    by_sender = recv.reshape(n_dp // 2, 2, half_rows, slice_width)
    other = jnp.sum(lax.dynamic_index_in_dim(by_sender, 1 - core, 1, keepdims=False), axis=0)
    got = lax.ppermute(other, "dp", core_swap)
    mine = jnp.sum(lax.dynamic_index_in_dim(by_sender, core, 1, keepdims=False), axis=0)
    total = jnp.where(
        core == 0, jnp.concatenate([mine, got], axis=0), jnp.concatenate([got, mine], axis=0)
    )
    me = lax.axis_index("dp")
    perm = []
    for src_s in range(n_dp):
        for src_m in range(n_t):
            o = (src_s // 2 - src_m) % n_t
            h = src_s % 2
            if win < o <= 2 * win:
                dst = ((src_s - 2 * win) % n_dp, (src_m - win) % n_t)
            elif o > 2 * win and o < n_t - win:
                dst = ((2 * (src_m - win) + h) % n_dp, (src_m + o - 2 * win) % n_t)
            else:
                continue
            perm.append((src_s * n_t + src_m, dst[0] * n_t + dst[1]))
    moved = lax.ppermute(total, ("dp", "tensor"), perm)
    my_o = (me // 2 - m) % n_t
    is_far = jnp.logical_and(my_o > win, my_o < n_t - win)
    final = jnp.where(is_far, moved, total)
    gram_cols = final[:col_width]
    mean_cols = final[col_width, :col_width] / token_total
    own_sums = stats[:, :slice_width]
    class_counts = stats[:, slice_width]
    mean_rows = jnp.sum(own_sums, axis=0) / token_total
    covariance = gram_cols.T / token_total - mean_rows[:, None] * mean_cols[None, :]
    cross_covariance = (own_sums - class_counts[:, None] * mean_rows[None, :]) / token_total
    return (covariance, cross_covariance)


def solution(mesh):
    in_specs = (P("dp", "tensor"), P("dp"))
    out_specs = (P("tensor", "dp"), P(None, "tensor"))
    return jax.shard_map(body, mesh=mesh, in_specs=in_specs, out_specs=out_specs, check_vma=False)
```
